32 devices in a mesh: dp: 2 (over x), expert: 4 (over y, core), tensor: 4 (over z).
Axes of the slice: x: 2, y: 2, z: 4, core: 2. Of those that a mesh axis runs over, the one named last changes fastest.
Arguments:
- output_grad: bfloat16 [2048, 4096], P(('dp', 'expert'), 'tensor'), may hold values from -6 to 6
- expert_ids: int32 [2048, 2], P(('dp', 'expert')), may hold values from 0 to 3, all different within a row; in each aligned block of 256 rows (0 to 255, 256 to 511, ...) at most 192 rows name the same one
- router_weights: bfloat16 [2048, 2], P(('dp', 'expert')), may hold values from 0.099609375 to 0.8984375
- gate_preact: bfloat16 [4, 1536, 14336], P('expert', 'dp', 'tensor'), may hold values from -6 to 6
- up_preact: bfloat16 [4, 1536, 14336], P('expert', 'dp', 'tensor'), may hold values from -6 to 6
- down_weight: bfloat16 [4, 14336, 4096], P('expert', 'tensor', 'dp'), may hold values from -0.046875 to 0.046875
Outputs:
- gate_preact_grad: bfloat16 [4, 1536, 14336], P('expert', 'dp', 'tensor')
- up_preact_grad: bfloat16 [4, 1536, 14336], P('expert', 'dp', 'tensor')
- down_grad: bfloat16 [4, 14336, 4096], P('expert', 'tensor', 'dp')
- router_grad: float32 [2048, 2], P(('dp', 'expert'))
The draws below stay inside these ranges and needn't reach their ends.
Inputs may be any that keep to these rules, and one draw needn't show every extreme that they name: `expert_ids`: the ids of one token differ. Among the 256 rows of one device no expert is named by more than 192 rows, and in every draw some expert is named by exactly 192 rows of some device.
All inputs are finite; a program needn't handle non-finite values.
Results may differ from the reference program's by a relative error of at most 0.007.
Values may be sent and summed in bfloat16 or wider, within the bound.
No kernel may reach another device: no remote copies, remote signals or barrier semaphores. Data moves between devices by JAX's collectives and lax.ppermute only.
A program may use at most 192 MiB of HBM per device.

```python
import math
import jax
import jax.numpy as jnp
import numpy as np
from jax import lax

D = 4096
FF = 14336
TOP = 2
TOK_DEV = 256
EXPERTS = 4
CAP = 192
TOKENS = 2048
SLOTS = 1536
N_DP = 2


def level_of(key, extent, shards, smallest, top_value):
    gain = 1.0
    for dim, parts in shards:
        heights = jax.random.uniform(jax.random.fold_in(jax.random.fold_in(key, 6), dim), (parts,), jnp.float32, smallest / len(shards), top_value / len(shards))
        gain = gain * jnp.repeat(jnp.exp(heights), extent[dim] // parts).reshape((-1,) + (1,) * (len(extent) - 1 - dim))
    return gain


def assign_block(rng, own, number, rows, count, top, most, skew):
    sequence = jax.random.permutation(rng, count)
    crowded, common = load_shares(count, rows * top, most, skew, True), load_shares(count, rows * top, most, skew, False)
    places = jnp.arange(count)

    def named(tallies, turn):
        used = int((tallies > 0).sum())
        fixed = max(1, used // 4)
        shifted = fixed + (places - fixed + turn * (used - fixed)) % max(1, count - fixed)
        return jnp.zeros((count,), jnp.int32).at[sequence[jnp.where(places < fixed, places, shifted)]].set(jnp.asarray(tallies, jnp.int32))

    tallies = jnp.where(number % 4 == 0, named(crowded, number // 4), named(common, number - number // 4 - 1))
    mixed = jax.random.permutation(jax.random.fold_in(own, 3), count)
    source_of, sink = mixed[0:count // 2 * 2:2], mixed[1:count // 2 * 2:2]
    margin = jnp.minimum(tallies[source_of] - 1, most - tallies[sink]) // 2
    margin = jnp.where((source_of == sequence[0]) | (sink == sequence[0]) | (tallies[sink] == 0), 0, jnp.maximum(margin, 0))
    shifted = jax.random.randint(jax.random.fold_in(own, 4), (count // 2,), 0, 1 << 20) % (margin + 1)
    tallies = tallies.at[source_of].add(-shifted).at[sink].add(shifted)
    members = jnp.searchsorted(jnp.cumsum(tallies), jnp.arange(rows * top), side="right").astype(jnp.int32)
    table = members.reshape(top, rows).T
    table = table[jax.random.permutation(jax.random.fold_in(own, 1), rows)]
    turn = jax.random.randint(jax.random.fold_in(own, 2), (rows, 1), 0, top)
    return jnp.take_along_axis(table, (jnp.arange(top)[None, :] + turn) % top, axis=1)


def load_shares(count, total, bound, skew, full):
    weights = [(1 << 20) // math.isqrt(grade ** skew) + 1 for grade in range(1, count + 1)]
    largest = bound if full else min(bound, max(-(-total // count), total * weights[0] // sum(weights)))
    least = 1 if total - largest >= count - 1 else 0
    counts, spare = [largest] + [least] * (count - 1), total - largest - least * (count - 1)
    while spare > 0:
        movable = [i for i in range(1, count) if counts[i] < largest] or [i for i in range(1, count) if counts[i] < bound]
        pool, left = sum([weights[i] for i in movable]), spare
        for i in movable:
            more = min(bound - counts[i], max(1, left * weights[i] // pool), spare)
            counts[i] = counts[i] + more
            spare = spare - more
    return np.array(counts)


def gaussian(stream_key, extent, width, most, split=(), held_as=jnp.bfloat16):
    result = width * jax.random.normal(stream_key, extent, jnp.float32)
    if split:
        result = result * level_of(stream_key, extent, split, -0.22, 0.18)
    return jnp.clip(result, -most, most).astype(held_as)


def setup_inputs(seed: int = 0) -> dict:
    seeds = jax.random.split(jax.random.key(seed), 7)
    output_grad = gaussian(seeds[0], (TOKENS, D), 1.0, 6.0, ((0, 8), (1, 4)))
    expert_ids_keys = jax.random.split(jax.random.fold_in(seeds[1], 1), TOKENS // TOK_DEV)
    expert_ids_turns = jax.random.permutation(jax.random.fold_in(seeds[1], 3), TOKENS // TOK_DEV)
    expert_ids = jax.vmap(lambda own, number: assign_block(jax.random.fold_in(seeds[1], 2), own, number, TOK_DEV, EXPERTS, TOP, CAP, 2))(expert_ids_keys, expert_ids_turns).reshape((TOKENS, TOP))
    router_weights = jnp.clip(0.099609375 + 0.7988281 * jax.random.uniform(seeds[2], (TOKENS, TOP), jnp.float32) ** level_of(seeds[2], (TOKENS, TOP), ((0, 8),), -0.2, 0.2), 0.099609375, 0.8984375).astype(jnp.bfloat16)
    gate_preact = gaussian(seeds[3], (EXPERTS, SLOTS, FF), 1.5, 6.0, ((0, 4), (1, 2), (2, 4)))
    up_preact = gaussian(seeds[4], (EXPERTS, SLOTS, FF), 1.0, 6.0, ((0, 4), (1, 2), (2, 4)))
    down_weight = gaussian(seeds[5], (EXPERTS, FF, D), FF ** -0.5, 0.046875, ((0, 4), (1, 4), (2, 2)))
    return {"output_grad": output_grad, "expert_ids": expert_ids, "router_weights": router_weights, "gate_preact": gate_preact, "up_preact": up_preact, "down_weight": down_weight}


def silu_parts(values):
    sigma = jax.nn.sigmoid(values)
    return values * sigma, sigma * (1.0 + values * (1.0 - sigma))


def positions(expert_ids):
    blocks = expert_ids.shape[0] // TOK_DEV
    flat_ids = expert_ids.reshape(blocks, TOK_DEV * TOP)
    one_hot = (flat_ids[..., None] == jnp.arange(EXPERTS, dtype=jnp.int32)).astype(jnp.int32)
    earlier = jnp.cumsum(one_hot, axis=1) - one_hot
    slot_index = jnp.sum(earlier * one_hot, axis=-1)
    offsets = (jnp.arange(blocks, dtype=jnp.int32) * CAP)[:, None]
    return (slot_index + offsets).reshape(expert_ids.shape).astype(jnp.int32)


def per_expert(packed):
    expert_rows, expert_gates, gate_in, up_in, weight = packed
    gate_float = gate_in.astype(jnp.float32)
    up_float = up_in.astype(jnp.float32)
    active, slope = silu_parts(gate_float)
    hidden = (active * up_float).astype(jnp.bfloat16)
    upstream = jnp.dot(expert_rows, weight.T, preferred_element_type=jnp.float32)
    gate_column = expert_gates.astype(jnp.float32)[:, None]
    scaled = (gate_column * expert_rows.astype(jnp.float32)).astype(jnp.bfloat16)
    hidden_runs = hidden.reshape(N_DP, SLOTS // N_DP, FF)
    scaled_runs = scaled.reshape(N_DP, SLOTS // N_DP, D)
    summed = jnp.zeros((FF, D), jnp.float32)
    for replica in range(N_DP):
        partial_grad = jnp.dot(hidden_runs[replica].T, scaled_runs[replica], preferred_element_type=jnp.float32)
        rounded = lax.optimization_barrier(partial_grad.astype(jnp.bfloat16))
        summed = summed + rounded.astype(jnp.float32)
    down_part = summed.astype(jnp.bfloat16)
    score = jnp.sum(hidden.astype(jnp.float32) * upstream, axis=1)
    hidden_grad = gate_column * upstream
    gate_grad = (hidden_grad * up_float * slope).astype(jnp.bfloat16)
    up_grad = (hidden_grad * active).astype(jnp.bfloat16)
    return gate_grad, up_grad, down_part, score


def reference(output_grad, expert_ids, router_weights, gate_preact, up_preact, down_weight):
    position = positions(expert_ids)
    destination = (expert_ids * SLOTS + position).reshape(-1).astype(jnp.int32)
    repeated = jnp.repeat(output_grad, TOP, axis=0)
    dispatched = jnp.zeros((EXPERTS * SLOTS, D), jnp.bfloat16).at[destination].set(repeated)
    dispatched = dispatched.reshape(EXPERTS, SLOTS, D)
    slot_gates = jnp.zeros((EXPERTS * SLOTS,), jnp.bfloat16).at[destination].set(router_weights.reshape(-1))
    slot_gates = slot_gates.reshape(EXPERTS, SLOTS)
    gate_grad, up_grad, down_grad, scores = lax.map(per_expert, (dispatched, slot_gates, gate_preact, up_preact, down_weight))
    router_grad = scores.reshape(-1)[destination].reshape(expert_ids.shape)
    return gate_grad, up_grad, down_grad, router_grad
```

```python
import jax
import jax.numpy as jnp
from jax import lax
from jax.sharding import PartitionSpec as P

PARTIAL_DTYPE = jnp.float32


def silu_parts(values):
    sigma = jax.nn.sigmoid(values)
    return (values * sigma, sigma * (1.0 + values * (1.0 - sigma)))


def swap_dp(value):
    return lax.ppermute(value, "dp", perm=[(0, 1), (1, 0)])


def local(output_grad, expert_ids, router_weights, gate_preact, up_preact, down_weight):
    expert_count = lax.axis_size("expert")
    tensor_count = lax.axis_size("tensor")
    replica = lax.axis_index("dp")
    part = lax.axis_index("tensor")
    tokens_here = expert_ids.shape[0]
    choices_each = expert_ids.shape[1]
    capacity = gate_preact.shape[1] // expert_count
    flat_ids = expert_ids.reshape(-1)
    one_hot = (flat_ids[:, None] == jnp.arange(expert_count, dtype=jnp.int32)).astype(jnp.int32)
    earlier = jnp.cumsum(one_hot, axis=0) - one_hot
    slot_index = jnp.sum(earlier * one_hot, axis=1)
    target = (flat_ids * capacity + slot_index).reshape(tokens_here, choices_each)
    columns = jnp.arange(expert_count * capacity, dtype=jnp.int32)
    matches = [target[:, which][:, None] == columns[None, :] for which in range(choices_each)]
    selector = jnp.zeros((tokens_here, expert_count * capacity), jnp.bfloat16)
    gate_table = jnp.zeros((tokens_here, expert_count * capacity), jnp.float32)
    for which in range(choices_each):
        selector = jnp.where(matches[which], jnp.bfloat16(1.0), selector)
        gate_table = jnp.where(
            matches[which], router_weights[:, which : which + 1].astype(jnp.float32), gate_table
        )
    gate_send = jnp.sum(gate_table, axis=0).astype(jnp.bfloat16).reshape(expert_count, capacity)

    gate_float = gate_preact[0].astype(jnp.float32)
    up_float = up_preact[0].astype(jnp.float32)
    active, slope = silu_parts(gate_float)
    hidden = (active * up_float).astype(jnp.bfloat16)

    contract_rows = (((0,), (0,)), ((), ()))
    contract_cols = (((1,), (1,)), ((), ()))
    outgoing = lax.dot_general(
        selector, output_grad, contract_rows, preferred_element_type=jnp.float32
    )
    outgoing = outgoing.astype(jnp.bfloat16).reshape(expert_count, capacity, -1)
    hidden, outgoing = lax.optimization_barrier((hidden, outgoing))
    hidden_other = swap_dp(hidden)
    received = lax.all_to_all(outgoing, "expert", split_axis=0, concat_axis=0, tiled=True)
    gate_slots = lax.all_to_all(gate_send, "expert", split_axis=0, concat_axis=0, tiled=True)
    slots = expert_count * capacity
    narrow_rows = received.reshape(slots, -1)
    gate_bf16 = gate_slots.reshape(-1)
    gate_column = gate_bf16.astype(jnp.float32)[:, None]
    fragment = lax.all_gather(narrow_rows, "tensor", axis=1, tiled=True)

    width = fragment.shape[1]
    half = width // 2
    piece = half // tensor_count
    own_rows = lax.dynamic_slice_in_dim(fragment, replica * half, half, axis=1)
    send_rows = lax.dynamic_slice_in_dim(
        fragment, (1 - replica) * half + part * piece, piece, axis=1
    )
    other_piece = swap_dp(send_rows)
    other_rows = lax.all_gather(other_piece, "tensor", axis=1, tiled=True)
    hidden_other, other_rows = lax.optimization_barrier((hidden_other, other_rows))
    other_gates = swap_dp(gate_bf16).astype(jnp.float32)[:, None]

    local_weight = down_weight[0]
    partial_other = lax.dot_general(
        other_rows, local_weight, contract_cols, preferred_element_type=jnp.float32
    )
    partial_back = swap_dp(partial_other.astype(PARTIAL_DTYPE)).astype(jnp.float32)
    partial_own = lax.dot_general(
        own_rows, local_weight, contract_cols, preferred_element_type=jnp.float32
    )

    scaled_own = (gate_column * own_rows.astype(jnp.float32)).astype(jnp.bfloat16)
    scaled_other = (other_gates * other_rows.astype(jnp.float32)).astype(jnp.bfloat16)
    grad_own = lax.dot_general(hidden, scaled_own, contract_rows, preferred_element_type=jnp.float32)
    grad_other = lax.dot_general(
        hidden_other, scaled_other, contract_rows, preferred_element_type=jnp.float32
    )
    rounded_own = lax.optimization_barrier(grad_own.astype(jnp.bfloat16))
    rounded_other = lax.optimization_barrier(grad_other.astype(jnp.bfloat16))
    partial_back, rounded_own, rounded_other = lax.optimization_barrier(
        (partial_back, rounded_own, rounded_other)
    )
    upstream = partial_own + partial_back
    down_grad = (rounded_own.astype(jnp.float32) + rounded_other.astype(jnp.float32)).astype(
        jnp.bfloat16
    )

    score = jnp.sum(hidden.astype(jnp.float32) * upstream, axis=1)
    hidden_grad = gate_column * upstream
    gate_grad = (hidden_grad * up_float * slope).astype(jnp.bfloat16)
    up_grad = (hidden_grad * active).astype(jnp.bfloat16)
    summed_scores = lax.psum(score, "tensor")
    returned = lax.all_to_all(
        summed_scores.reshape(expert_count, capacity),
        "expert",
        split_axis=0,
        concat_axis=0,
        tiled=True,
    )
    flat_scores = returned.reshape(-1)
    router_grad = jnp.stack(
        [
            jnp.sum(jnp.where(matches[which], flat_scores[None, :], 0.0), axis=1)
            for which in range(choices_each)
        ],
        axis=1,
    )
    return (gate_grad[None], up_grad[None], down_grad[None], router_grad)


def solution(mesh):
    placed = (
        P(("dp", "expert"), "tensor"),
        P(("dp", "expert"), None),
        P(("dp", "expert"), None),
        P("expert", "dp", "tensor"),
        P("expert", "dp", "tensor"),
        P("expert", "tensor", "dp"),
    )
    return jax.shard_map(
        local,
        mesh=mesh,
        in_specs=placed,
        out_specs=(
            P("expert", "dp", "tensor"),
            P("expert", "dp", "tensor"),
            P("expert", "tensor", "dp"),
            P(("dp", "expert"), None),
        ),
        check_vma=False,
    )
```

```python
import jax
import jax.numpy as jnp
from jax import lax
from jax.sharding import PartitionSpec as P

PARTIAL_DTYPE = jnp.bfloat16


def silu_parts(values):
    sigma = jax.nn.sigmoid(values)
    return (values * sigma, sigma * (1.0 + values * (1.0 - sigma)))


def swap_dp(value):
    return lax.ppermute(value, "dp", perm=[(0, 1), (1, 0)])


def local(output_grad, expert_ids, router_weights, gate_preact, up_preact, down_weight):
    expert_count = lax.axis_size("expert")
    tensor_count = lax.axis_size("tensor")
    replica = lax.axis_index("dp")
    part = lax.axis_index("tensor")
    tokens_here = expert_ids.shape[0]
    choices_each = expert_ids.shape[1]
    capacity = gate_preact.shape[1] // expert_count
    flat_ids = expert_ids.reshape(-1)
    one_hot = (flat_ids[:, None] == jnp.arange(expert_count, dtype=jnp.int32)).astype(jnp.int32)
    earlier = jnp.cumsum(one_hot, axis=0) - one_hot
    slot_index = jnp.sum(earlier * one_hot, axis=1)
    target = (flat_ids * capacity + slot_index).reshape(tokens_here, choices_each)
    columns = jnp.arange(expert_count * capacity, dtype=jnp.int32)
    matches = [target[:, which][:, None] == columns[None, :] for which in range(choices_each)]
    selector = jnp.zeros((tokens_here, expert_count * capacity), jnp.bfloat16)
    gate_table = jnp.zeros((tokens_here, expert_count * capacity), jnp.float32)
    for which in range(choices_each):
        selector = jnp.where(matches[which], jnp.bfloat16(1.0), selector)
        gate_table = jnp.where(
            matches[which], router_weights[:, which : which + 1].astype(jnp.float32), gate_table
        )
    gate_send = jnp.sum(gate_table, axis=0).astype(jnp.bfloat16).reshape(expert_count, capacity)

    gate_float = gate_preact[0].astype(jnp.float32)
    up_float = up_preact[0].astype(jnp.float32)
    active, slope = silu_parts(gate_float)
    hidden = (active * up_float).astype(jnp.bfloat16)

    contract_rows = (((0,), (0,)), ((), ()))
    contract_cols = (((1,), (1,)), ((), ()))
    outgoing = lax.dot_general(
        selector, output_grad, contract_rows, preferred_element_type=jnp.float32
    )
    outgoing = outgoing.astype(jnp.bfloat16).reshape(expert_count, capacity, -1)
    hidden, outgoing, gate_send = lax.optimization_barrier((hidden, outgoing, gate_send))
    hidden_other = swap_dp(hidden)
    gate_slots = lax.all_to_all(gate_send, "expert", split_axis=0, concat_axis=0, tiled=True)
    received = lax.all_to_all(outgoing, "expert", split_axis=0, concat_axis=0, tiled=True)
    slots = expert_count * capacity
    narrow_rows = received.reshape(slots, -1)
    gate_bf16 = gate_slots.reshape(-1)
    gate_column = gate_bf16.astype(jnp.float32)[:, None]
    other_gates = swap_dp(gate_bf16)
    fragment = lax.all_gather(narrow_rows, "tensor", axis=1, tiled=True)

    width = fragment.shape[1]
    half = width // 2
    piece = half // tensor_count
    own_rows = lax.dynamic_slice_in_dim(fragment, replica * half, half, axis=1)
    send_rows = lax.dynamic_slice_in_dim(
        fragment, (1 - replica) * half + part * piece, piece, axis=1
    )
    other_piece = swap_dp(send_rows)
    other_rows = lax.all_gather(other_piece, "tensor", axis=1, tiled=True)
    hidden_other, other_rows, other_gates = lax.optimization_barrier(
        (hidden_other, other_rows, other_gates)
    )
    other_gates = other_gates.astype(jnp.float32)[:, None]

    local_weight = down_weight[0]
    partial_other = lax.dot_general(
        other_rows, local_weight, contract_cols, preferred_element_type=jnp.float32
    )
    partial_back = swap_dp(partial_other.astype(PARTIAL_DTYPE)).astype(jnp.float32)
    partial_own = lax.dot_general(
        own_rows, local_weight, contract_cols, preferred_element_type=jnp.float32
    )

    scaled_own = (gate_column * own_rows.astype(jnp.float32)).astype(jnp.bfloat16)
    scaled_other = (other_gates * other_rows.astype(jnp.float32)).astype(jnp.bfloat16)
    grad_own = lax.dot_general(hidden, scaled_own, contract_rows, preferred_element_type=jnp.float32)
    grad_other = lax.dot_general(
        hidden_other, scaled_other, contract_rows, preferred_element_type=jnp.float32
    )
    rounded_own = lax.optimization_barrier(grad_own.astype(jnp.bfloat16))
    rounded_other = lax.optimization_barrier(grad_other.astype(jnp.bfloat16))
    down_grad = (rounded_own.astype(jnp.float32) + rounded_other.astype(jnp.float32)).astype(
        jnp.bfloat16
    )
    partial_back, partial_own, down_grad = lax.optimization_barrier(
        (partial_back, partial_own, down_grad)
    )
    upstream = partial_own + partial_back

    score = jnp.sum(hidden.astype(jnp.float32) * upstream, axis=1)
    hidden_grad = gate_column * upstream
    gate_grad = (hidden_grad * up_float * slope).astype(jnp.bfloat16)
    up_grad = (hidden_grad * active).astype(jnp.bfloat16)
    summed_scores = lax.psum(score, "tensor")
    returned = lax.all_to_all(
        summed_scores.reshape(expert_count, capacity),
        "expert",
        split_axis=0,
        concat_axis=0,
        tiled=True,
    )
    flat_scores = returned.reshape(-1)
    router_grad = jnp.stack(
        [
            jnp.sum(jnp.where(matches[which], flat_scores[None, :], 0.0), axis=1)
            for which in range(choices_each)
        ],
        axis=1,
    )
    return (gate_grad[None], up_grad[None], down_grad[None], router_grad)


def solution(mesh):
    placed = (
        P(("dp", "expert"), "tensor"),
        P(("dp", "expert"), None),
        P(("dp", "expert"), None),
        P("expert", "dp", "tensor"),
        P("expert", "dp", "tensor"),
        P("expert", "tensor", "dp"),
    )
    return jax.shard_map(
        local,
        mesh=mesh,
        in_specs=placed,
        out_specs=(
            P("expert", "dp", "tensor"),
            P("expert", "dp", "tensor"),
            P("expert", "tensor", "dp"),
            P(("dp", "expert"), None),
        ),
        check_vma=False,
    )
```

```python
import jax
import jax.numpy as jnp
from jax import lax
from jax.sharding import PartitionSpec as P

PARTIAL_DTYPE = jnp.bfloat16
CHUNKS = 2


def silu_parts(values):
    sigma = jax.nn.sigmoid(values)
    return (values * sigma, sigma * (1.0 + values * (1.0 - sigma)))


def swap_dp(value):
    return lax.ppermute(value, "dp", perm=[(0, 1), (1, 0)])


def local(output_grad, expert_ids, router_weights, gate_preact, up_preact, down_weight):
    expert_count = lax.axis_size("expert")
    tensor_count = lax.axis_size("tensor")
    replica = lax.axis_index("dp")
    part = lax.axis_index("tensor")
    tokens_here = expert_ids.shape[0]
    choices_each = expert_ids.shape[1]
    capacity = gate_preact.shape[1] // expert_count
    flat_ids = expert_ids.reshape(-1)
    one_hot = (flat_ids[:, None] == jnp.arange(expert_count, dtype=jnp.int32)).astype(jnp.int32)
    earlier = jnp.cumsum(one_hot, axis=0) - one_hot
    slot_index = jnp.sum(earlier * one_hot, axis=1)
    target = (flat_ids * capacity + slot_index).reshape(tokens_here, choices_each)
    columns = jnp.arange(expert_count * capacity, dtype=jnp.int32)
    matches = [target[:, which][:, None] == columns[None, :] for which in range(choices_each)]
    selector = jnp.zeros((tokens_here, expert_count * capacity), jnp.bfloat16)
    gate_table = jnp.zeros((tokens_here, expert_count * capacity), jnp.float32)
    for which in range(choices_each):
        selector = jnp.where(matches[which], jnp.bfloat16(1.0), selector)
        gate_table = jnp.where(
            matches[which], router_weights[:, which : which + 1].astype(jnp.float32), gate_table
        )
    gate_send = jnp.sum(gate_table, axis=0).astype(jnp.bfloat16).reshape(expert_count, capacity)

    gate_float = gate_preact[0].astype(jnp.float32)
    up_float = up_preact[0].astype(jnp.float32)
    active, slope = silu_parts(gate_float)
    hidden = (active * up_float).astype(jnp.bfloat16)

    contract_rows = (((0,), (0,)), ((), ()))
    contract_cols = (((1,), (1,)), ((), ()))
    outgoing = lax.dot_general(
        selector, output_grad, contract_rows, preferred_element_type=jnp.float32
    )
    outgoing = outgoing.astype(jnp.bfloat16).reshape(expert_count, capacity, -1)
    hidden, outgoing, gate_send = lax.optimization_barrier((hidden, outgoing, gate_send))
    gate_slots = lax.all_to_all(gate_send, "expert", split_axis=0, concat_axis=0, tiled=True)
    received = lax.all_to_all(outgoing, "expert", split_axis=0, concat_axis=0, tiled=True)
    slots = expert_count * capacity
    narrow_rows = received.reshape(slots, -1)
    gate_bf16 = gate_slots.reshape(-1)
    gate_column = gate_bf16.astype(jnp.float32)[:, None]
    other_gates = swap_dp(gate_bf16)
    width = narrow_rows.shape[1] * tensor_count
    half = width // 2
    piece = half // tensor_count
    local_weight = down_weight[0]
    chunk = slots // CHUNKS
    hidden_parts = [swap_dp(hidden[:chunk])]
    fragments = [
        lax.all_gather(narrow_rows[index * chunk : (index + 1) * chunk], "tensor", axis=1, tiled=True)
        for index in range(CHUNKS)
    ]
    own_parts = [
        lax.dynamic_slice_in_dim(fragment, replica * half, half, axis=1) for fragment in fragments
    ]
    pieces = []
    for index in range(CHUNKS):
        send_rows = lax.dynamic_slice_in_dim(
            fragments[index], (1 - replica) * half + part * piece, piece, axis=1
        )
        send_rows, hidden_parts[-1] = lax.optimization_barrier((send_rows, hidden_parts[-1]))
        pieces.append(swap_dp(send_rows))
        if index + 1 < CHUNKS:
            next_hidden, pieces[-1] = lax.optimization_barrier(
                (hidden[(index + 1) * chunk : (index + 2) * chunk], pieces[-1])
            )
            hidden_parts.append(swap_dp(next_hidden))
    other_parts, partial_own_parts, partial_back_parts = [], [], []
    for index in range(CHUNKS):
        other_part = lax.all_gather(pieces[index], "tensor", axis=1, tiled=True)
        if index == 0:
            other_part, pieces[-1] = lax.optimization_barrier((other_part, pieces[-1]))
        other_parts.append(other_part)
        partial_other = lax.dot_general(
            other_part, local_weight, contract_cols, preferred_element_type=jnp.float32
        )
        partial_back_parts.append(swap_dp(partial_other.astype(PARTIAL_DTYPE)))
        partial_own_parts.append(
            lax.dot_general(
                own_parts[index], local_weight, contract_cols, preferred_element_type=jnp.float32
            )
        )
    hidden_other = jnp.concatenate(hidden_parts, axis=0)
    own_rows = jnp.concatenate(own_parts, axis=0)
    other_rows = jnp.concatenate(other_parts, axis=0)
    partial_own = jnp.concatenate(partial_own_parts, axis=0)
    partial_back = jnp.concatenate(partial_back_parts, axis=0).astype(jnp.float32)
    hidden_other, other_rows, other_gates = lax.optimization_barrier(
        (hidden_other, other_rows, other_gates)
    )
    other_gates = other_gates.astype(jnp.float32)[:, None]

    scaled_own = (gate_column * own_rows.astype(jnp.float32)).astype(jnp.bfloat16)
    scaled_other = (other_gates * other_rows.astype(jnp.float32)).astype(jnp.bfloat16)
    grad_own = lax.dot_general(hidden, scaled_own, contract_rows, preferred_element_type=jnp.float32)
    grad_other = lax.dot_general(
        hidden_other, scaled_other, contract_rows, preferred_element_type=jnp.float32
    )
    rounded_own = lax.optimization_barrier(grad_own.astype(jnp.bfloat16))
    rounded_other = lax.optimization_barrier(grad_other.astype(jnp.bfloat16))
    down_grad = (rounded_own.astype(jnp.float32) + rounded_other.astype(jnp.float32)).astype(
        jnp.bfloat16
    )
    partial_back, partial_own, down_grad = lax.optimization_barrier(
        (partial_back, partial_own, down_grad)
    )
    upstream = partial_own + partial_back

    score = jnp.sum(hidden.astype(jnp.float32) * upstream, axis=1)
    hidden_grad = gate_column * upstream
    gate_grad = (hidden_grad * up_float * slope).astype(jnp.bfloat16)
    up_grad = (hidden_grad * active).astype(jnp.bfloat16)
    summed_scores = lax.psum(score, "tensor")
    returned = lax.all_to_all(
        summed_scores.reshape(expert_count, capacity),
        "expert",
        split_axis=0,
        concat_axis=0,
        tiled=True,
    )
    flat_scores = returned.reshape(-1)
    router_grad = jnp.stack(
        [
            jnp.sum(jnp.where(matches[which], flat_scores[None, :], 0.0), axis=1)
            for which in range(choices_each)
        ],
        axis=1,
    )
    return (gate_grad[None], up_grad[None], down_grad[None], router_grad)


def solution(mesh):
    placed = (
        P(("dp", "expert"), "tensor"),
        P(("dp", "expert"), None),
        P(("dp", "expert"), None),
        P("expert", "dp", "tensor"),
        P("expert", "dp", "tensor"),
        P("expert", "tensor", "dp"),
    )
    return jax.shard_map(
        local,
        mesh=mesh,
        in_specs=placed,
        out_specs=(
            P("expert", "dp", "tensor"),
            P("expert", "dp", "tensor"),
            P("expert", "tensor", "dp"),
            P(("dp", "expert"), None),
        ),
        check_vma=False,
    )
```

```python
import jax
import jax.numpy as jnp
from jax import lax
from jax.sharding import PartitionSpec as P

PARTIAL_DTYPE = jnp.bfloat16


def silu_parts(values):
    sigma = jax.nn.sigmoid(values)
    return (values * sigma, sigma * (1.0 + values * (1.0 - sigma)))


def swap_dp(value):
    return lax.ppermute(value, "dp", perm=[(0, 1), (1, 0)])


def local(output_grad, expert_ids, router_weights, gate_preact, up_preact, down_weight):
    expert_count = lax.axis_size("expert")
    tensor_count = lax.axis_size("tensor")
    replica = lax.axis_index("dp")
    part = lax.axis_index("tensor")
    tokens_here = expert_ids.shape[0]
    choices_each = expert_ids.shape[1]
    capacity = gate_preact.shape[1] // expert_count
    flat_ids = expert_ids.reshape(-1)
    one_hot = (flat_ids[:, None] == jnp.arange(expert_count, dtype=jnp.int32)).astype(jnp.int32)
    earlier = jnp.cumsum(one_hot, axis=0) - one_hot
    slot_index = jnp.sum(earlier * one_hot, axis=1)
    target = (flat_ids * capacity + slot_index).reshape(tokens_here, choices_each)
    columns = jnp.arange(expert_count * capacity, dtype=jnp.int32)
    matches = [target[:, which][:, None] == columns[None, :] for which in range(choices_each)]
    selector = jnp.zeros((tokens_here, expert_count * capacity), jnp.bfloat16)
    gate_table = jnp.zeros((tokens_here, expert_count * capacity), jnp.float32)
    for which in range(choices_each):
        selector = jnp.where(matches[which], jnp.bfloat16(1.0), selector)
        gate_table = jnp.where(
            matches[which], router_weights[:, which : which + 1].astype(jnp.float32), gate_table
        )
    gate_send = jnp.sum(gate_table, axis=0).astype(jnp.bfloat16).reshape(expert_count, capacity)

    local_weight = down_weight[0]
    units = local_weight.shape[0]
    moved = units // 4 // 16 * 16

    gate_float = gate_preact[0].astype(jnp.float32)
    up_float = up_preact[0].astype(jnp.float32)
    active, slope = silu_parts(gate_float)
    hidden = (active * up_float).astype(jnp.bfloat16)

    contract_rows = (((0,), (0,)), ((), ()))
    contract_cols = (((1,), (1,)), ((), ()))
    outgoing = lax.dot_general(
        selector, output_grad, contract_rows, preferred_element_type=jnp.float32
    )
    outgoing = outgoing.astype(jnp.bfloat16).reshape(expert_count, capacity, -1)
    hidden, outgoing, gate_send = lax.optimization_barrier((hidden, outgoing, gate_send))
    hidden_other = swap_dp(hidden)
    gate_slots = lax.all_to_all(gate_send, "expert", split_axis=0, concat_axis=0, tiled=True)
    received = lax.all_to_all(outgoing, "expert", split_axis=0, concat_axis=0, tiled=True)
    slots = expert_count * capacity
    narrow_rows = received.reshape(slots, -1)
    gate_bf16 = gate_slots.reshape(-1)
    gate_column = gate_bf16.astype(jnp.float32)[:, None]
    other_gates = swap_dp(gate_bf16)
    fragment = lax.all_gather(narrow_rows, "tensor", axis=1, tiled=True)
    fragment, hidden_other = lax.optimization_barrier((fragment, hidden_other))

    width = fragment.shape[1]
    half = width // 2
    piece = half // tensor_count
    own_rows = lax.dynamic_slice_in_dim(fragment, replica * half, half, axis=1)
    send_rows = lax.dynamic_slice_in_dim(
        fragment, (1 - replica) * half + part * piece, piece, axis=1
    )
    other_piece = swap_dp(send_rows)
    weight_rest, other_piece = lax.optimization_barrier((local_weight[:moved], other_piece))
    weight_moved = swap_dp(weight_rest)
    other_rows = lax.all_gather(other_piece, "tensor", axis=1, tiled=True)
    hidden_other, other_rows, other_gates = lax.optimization_barrier(
        (hidden_other, other_rows, other_gates)
    )
    other_gates = other_gates.astype(jnp.float32)[:, None]

    partial_other = lax.dot_general(
        other_rows, local_weight[moved:], contract_cols, preferred_element_type=jnp.float32
    )
    weight_moved, partial_send = lax.optimization_barrier(
        (weight_moved, partial_other.astype(PARTIAL_DTYPE))
    )
    partial_back = swap_dp(partial_send).astype(jnp.float32)
    partial_own = lax.dot_general(
        own_rows, local_weight, contract_cols, preferred_element_type=jnp.float32
    )
    far_rows = lax.dynamic_slice_in_dim(fragment, (1 - replica) * half, half, axis=1)
    near = lax.dot_general(far_rows, weight_moved, contract_cols, preferred_element_type=jnp.float32)

    scaled_own = (gate_column * own_rows.astype(jnp.float32)).astype(jnp.bfloat16)
    scaled_other = (other_gates * other_rows.astype(jnp.float32)).astype(jnp.bfloat16)
    grad_own = lax.dot_general(hidden, scaled_own, contract_rows, preferred_element_type=jnp.float32)
    grad_other = lax.dot_general(
        hidden_other, scaled_other, contract_rows, preferred_element_type=jnp.float32
    )
    rounded_own = lax.optimization_barrier(grad_own.astype(jnp.bfloat16))
    rounded_other = lax.optimization_barrier(grad_other.astype(jnp.bfloat16))
    down_grad = (rounded_own.astype(jnp.float32) + rounded_other.astype(jnp.float32)).astype(
        jnp.bfloat16
    )
    partial_back, partial_own, near, down_grad = lax.optimization_barrier(
        (partial_back, partial_own, near, down_grad)
    )
    upstream = partial_own + jnp.concatenate((near, partial_back), axis=1)

    score = jnp.sum(hidden.astype(jnp.float32) * upstream, axis=1)
    hidden_grad = gate_column * upstream
    gate_grad = (hidden_grad * up_float * slope).astype(jnp.bfloat16)
    up_grad = (hidden_grad * active).astype(jnp.bfloat16)
    summed_scores = lax.psum(score, "tensor")
    returned = lax.all_to_all(
        summed_scores.reshape(expert_count, capacity),
        "expert",
        split_axis=0,
        concat_axis=0,
        tiled=True,
    )
    flat_scores = returned.reshape(-1)
    router_grad = jnp.stack(
        [
            jnp.sum(jnp.where(matches[which], flat_scores[None, :], 0.0), axis=1)
            for which in range(choices_each)
        ],
        axis=1,
    )
    return (gate_grad[None], up_grad[None], down_grad[None], router_grad)


def solution(mesh):
    placed = (
        P(("dp", "expert"), "tensor"),
        P(("dp", "expert"), None),
        P(("dp", "expert"), None),
        P("expert", "dp", "tensor"),
        P("expert", "dp", "tensor"),
        P("expert", "tensor", "dp"),
    )
    return jax.shard_map(
        local,
        mesh=mesh,
        in_specs=placed,
        out_specs=(
            P("expert", "dp", "tensor"),
            P("expert", "dp", "tensor"),
            P("expert", "tensor", "dp"),
            P(("dp", "expert"), None),
        ),
        check_vma=False,
    )
```

```python
import jax
import jax.numpy as jnp
from jax import lax
from jax.sharding import PartitionSpec as P

PARTIAL_DTYPE = jnp.bfloat16


def silu_parts(values):
    sigma = jax.nn.sigmoid(values)
    return (values * sigma, sigma * (1.0 + values * (1.0 - sigma)))


def swap_dp(value):
    return lax.ppermute(value, "dp", perm=[(0, 1), (1, 0)])


def local(output_grad, expert_ids, router_weights, gate_preact, up_preact, down_weight):
    expert_count = lax.axis_size("expert")
    tensor_count = lax.axis_size("tensor")
    replica = lax.axis_index("dp")
    part = lax.axis_index("tensor")
    tokens_here = expert_ids.shape[0]
    choices_each = expert_ids.shape[1]
    capacity = gate_preact.shape[1] // expert_count
    flat_ids = expert_ids.reshape(-1)
    one_hot = (flat_ids[:, None] == jnp.arange(expert_count, dtype=jnp.int32)).astype(jnp.int32)
    earlier = jnp.cumsum(one_hot, axis=0) - one_hot
    slot_index = jnp.sum(earlier * one_hot, axis=1)
    target = (flat_ids * capacity + slot_index).reshape(tokens_here, choices_each)
    columns = jnp.arange(expert_count * capacity, dtype=jnp.int32)
    matches = [target[:, which][:, None] == columns[None, :] for which in range(choices_each)]
    selector = jnp.zeros((tokens_here, expert_count * capacity), jnp.bfloat16)
    gate_table = jnp.zeros((tokens_here, expert_count * capacity), jnp.float32)
    for which in range(choices_each):
        selector = jnp.where(matches[which], jnp.bfloat16(1.0), selector)
        gate_table = jnp.where(
            matches[which], router_weights[:, which : which + 1].astype(jnp.float32), gate_table
        )
    gate_send = jnp.sum(gate_table, axis=0).astype(jnp.bfloat16).reshape(expert_count, capacity)

    local_weight = down_weight[0]
    units = local_weight.shape[0]
    moved = units // 4 // 16 * 16

    gate_float = gate_preact[0].astype(jnp.float32)
    up_float = up_preact[0].astype(jnp.float32)
    active, slope = silu_parts(gate_float)
    hidden = (active * up_float).astype(jnp.bfloat16)

    contract_rows = (((0,), (0,)), ((), ()))
    contract_cols = (((1,), (1,)), ((), ()))
    outgoing = lax.dot_general(
        selector, output_grad, contract_rows, preferred_element_type=jnp.float32
    )
    outgoing = outgoing.astype(jnp.bfloat16).reshape(expert_count, capacity, -1)
    hidden, outgoing, gate_send = lax.optimization_barrier((hidden, outgoing, gate_send))
    hidden_other = swap_dp(hidden)
    gate_slots = lax.all_to_all(gate_send, "expert", split_axis=0, concat_axis=0, tiled=True)
    received = lax.all_to_all(outgoing, "expert", split_axis=0, concat_axis=0, tiled=True)
    slots = expert_count * capacity
    narrow_rows = received.reshape(slots, -1)
    gate_bf16 = gate_slots.reshape(-1)
    gate_column = gate_bf16.astype(jnp.float32)[:, None]
    other_gates = swap_dp(gate_bf16)
    fragment = lax.all_gather(narrow_rows, "tensor", axis=1, tiled=True)
    fragment, hidden_other, other_gates = lax.optimization_barrier(
        (fragment, hidden_other, other_gates)
    )

    width = fragment.shape[1]
    half = width // 2
    piece = half // tensor_count
    own_rows = lax.dynamic_slice_in_dim(fragment, replica * half, half, axis=1)
    send_rows = lax.dynamic_slice_in_dim(
        fragment, (1 - replica) * half + part * piece, piece, axis=1
    )
    other_piece = swap_dp(send_rows)
    weight_rest, other_piece = lax.optimization_barrier((local_weight[:moved], other_piece))
    weight_moved = swap_dp(weight_rest)
    other_rows = lax.all_gather(other_piece, "tensor", axis=1, tiled=True)
    hidden_other, other_rows = lax.optimization_barrier((hidden_other, other_rows))
    other_gates = other_gates.astype(jnp.float32)[:, None]

    partial_other = lax.dot_general(
        other_rows, local_weight[moved:], contract_cols, preferred_element_type=jnp.float32
    )
    weight_moved, partial_send, own_rows = lax.optimization_barrier(
        (weight_moved, partial_other.astype(PARTIAL_DTYPE), own_rows)
    )
    partial_back = swap_dp(partial_send).astype(jnp.float32)
    partial_own = lax.dot_general(
        own_rows, local_weight, contract_cols, preferred_element_type=jnp.float32
    )
    far_rows = lax.dynamic_slice_in_dim(fragment, (1 - replica) * half, half, axis=1)
    near = lax.dot_general(far_rows, weight_moved, contract_cols, preferred_element_type=jnp.float32)

    scaled_own = (gate_column * own_rows.astype(jnp.float32)).astype(jnp.bfloat16)
    scaled_other = (other_gates * other_rows.astype(jnp.float32)).astype(jnp.bfloat16)
    grad_own = lax.dot_general(hidden, scaled_own, contract_rows, preferred_element_type=jnp.float32)
    grad_other = lax.dot_general(
        hidden_other, scaled_other, contract_rows, preferred_element_type=jnp.float32
    )
    rounded_own = lax.optimization_barrier(grad_own.astype(jnp.bfloat16))
    rounded_other = lax.optimization_barrier(grad_other.astype(jnp.bfloat16))
    down_grad = (rounded_own.astype(jnp.float32) + rounded_other.astype(jnp.float32)).astype(
        jnp.bfloat16
    )
    partial_back, partial_own, near, down_grad = lax.optimization_barrier(
        (partial_back, partial_own, near, down_grad)
    )
    upstream = partial_own + jnp.concatenate((near, partial_back), axis=1)

    score = jnp.sum(hidden.astype(jnp.float32) * upstream, axis=1)
    hidden_grad = gate_column * upstream
    gate_grad = (hidden_grad * up_float * slope).astype(jnp.bfloat16)
    up_grad = (hidden_grad * active).astype(jnp.bfloat16)
    summed_scores = lax.psum(score, "tensor")
    returned = lax.all_to_all(
        summed_scores.reshape(expert_count, capacity),
        "expert",
        split_axis=0,
        concat_axis=0,
        tiled=True,
    )
    flat_scores = returned.reshape(-1)
    router_grad = jnp.stack(
        [
            jnp.sum(jnp.where(matches[which], flat_scores[None, :], 0.0), axis=1)
            for which in range(choices_each)
        ],
        axis=1,
    )
    return (gate_grad[None], up_grad[None], down_grad[None], router_grad)


def solution(mesh):
    placed = (
        P(("dp", "expert"), "tensor"),
        P(("dp", "expert"), None),
        P(("dp", "expert"), None),
        P("expert", "dp", "tensor"),
        P("expert", "dp", "tensor"),
        P("expert", "tensor", "dp"),
    )
    return jax.shard_map(
        local,
        mesh=mesh,
        in_specs=placed,
        out_specs=(
            P("expert", "dp", "tensor"),
            P("expert", "dp", "tensor"),
            P("expert", "tensor", "dp"),
            P(("dp", "expert"), None),
        ),
        check_vma=False,
    )
```

```python
import jax
import jax.numpy as jnp
from jax import lax
from jax.sharding import PartitionSpec as P

PARTIAL_DTYPE = jnp.bfloat16


def silu_parts(values):
    sigma = jax.nn.sigmoid(values)
    return (values * sigma, sigma * (1.0 + values * (1.0 - sigma)))


def swap_dp(value):
    return lax.ppermute(value, "dp", perm=[(0, 1), (1, 0)])


def local(output_grad, expert_ids, router_weights, gate_preact, up_preact, down_weight):
    expert_count = lax.axis_size("expert")
    tensor_count = lax.axis_size("tensor")
    replica = lax.axis_index("dp")
    part = lax.axis_index("tensor")
    tokens_here = expert_ids.shape[0]
    choices_each = expert_ids.shape[1]
    capacity = gate_preact.shape[1] // expert_count
    flat_ids = expert_ids.reshape(-1)
    one_hot = (flat_ids[:, None] == jnp.arange(expert_count, dtype=jnp.int32)).astype(jnp.int32)
    earlier = jnp.cumsum(one_hot, axis=0) - one_hot
    slot_index = jnp.sum(earlier * one_hot, axis=1)
    target = (flat_ids * capacity + slot_index).reshape(tokens_here, choices_each)
    columns = jnp.arange(expert_count * capacity, dtype=jnp.int32)
    matches = [target[:, which][:, None] == columns[None, :] for which in range(choices_each)]
    selector = jnp.zeros((tokens_here, expert_count * capacity), jnp.bfloat16)
    gate_table = jnp.zeros((tokens_here, expert_count * capacity), jnp.float32)
    for which in range(choices_each):
        selector = jnp.where(matches[which], jnp.bfloat16(1.0), selector)
        gate_table = jnp.where(
            matches[which], router_weights[:, which : which + 1].astype(jnp.float32), gate_table
        )
    gate_send = jnp.sum(gate_table, axis=0).astype(jnp.bfloat16).reshape(expert_count, capacity)

    local_weight = down_weight[0]
    units = local_weight.shape[0]
    moved = units // 4 // 16 * 16

    gate_float = gate_preact[0].astype(jnp.float32)
    up_float = up_preact[0].astype(jnp.float32)
    active, slope = silu_parts(gate_float)
    hidden = (active * up_float).astype(jnp.bfloat16)

    contract_rows = (((0,), (0,)), ((), ()))
    contract_cols = (((1,), (1,)), ((), ()))
    outgoing = lax.dot_general(
        selector, output_grad, contract_rows, preferred_element_type=jnp.float32
    )
    outgoing = outgoing.astype(jnp.bfloat16).reshape(expert_count, capacity, -1)
    hidden, outgoing, gate_send = lax.optimization_barrier((hidden, outgoing, gate_send))
    hidden_other = swap_dp(hidden)
    gate_slots = lax.all_to_all(gate_send, "expert", split_axis=0, concat_axis=0, tiled=True)
    received = lax.all_to_all(outgoing, "expert", split_axis=0, concat_axis=0, tiled=True)
    slots = expert_count * capacity
    narrow_rows = received.reshape(slots, -1)
    gate_bf16 = gate_slots.reshape(-1)
    gate_column = gate_bf16.astype(jnp.float32)[:, None]
    other_gates = swap_dp(gate_bf16)
    fragment = lax.all_gather(narrow_rows, "tensor", axis=1, tiled=True)
    fragment, hidden_other, other_gates = lax.optimization_barrier(
        (fragment, hidden_other, other_gates)
    )

    width = fragment.shape[1]
    half = width // 2
    piece = half // tensor_count
    own_rows = lax.dynamic_slice_in_dim(fragment, replica * half, half, axis=1)
    send_rows = lax.dynamic_slice_in_dim(
        fragment, (1 - replica) * half + part * piece, piece, axis=1
    )
    other_piece = swap_dp(send_rows)
    weight_rest, other_piece = lax.optimization_barrier((local_weight[:moved], other_piece))
    weight_moved = swap_dp(weight_rest)
    other_rows = lax.all_gather(other_piece, "tensor", axis=1, tiled=True)
    hidden_other, other_rows = lax.optimization_barrier((hidden_other, other_rows))
    other_gates = other_gates.astype(jnp.float32)[:, None]

    partial_other = lax.dot_general(
        other_rows, local_weight[moved:], contract_cols, preferred_element_type=jnp.float32
    )
    weight_moved, partial_send, own_rows = lax.optimization_barrier(
        (weight_moved, partial_other.astype(PARTIAL_DTYPE), own_rows)
    )
    partial_back = swap_dp(partial_send).astype(jnp.float32)
    partial_own = lax.dot_general(
        own_rows, local_weight, contract_cols, preferred_element_type=jnp.float32
    )
    far_rows = lax.dynamic_slice_in_dim(fragment, (1 - replica) * half, half, axis=1)
    near = lax.dot_general(far_rows, weight_moved, contract_cols, preferred_element_type=jnp.float32)

    scaled_own = (gate_column * own_rows.astype(jnp.float32)).astype(jnp.bfloat16)
    scaled_other = (other_gates * other_rows.astype(jnp.float32)).astype(jnp.bfloat16)
    grad_own = lax.dot_general(hidden, scaled_own, contract_rows, preferred_element_type=jnp.float32)
    grad_other = lax.dot_general(
        hidden_other, scaled_other, contract_rows, preferred_element_type=jnp.float32
    )
    rounded_own = lax.optimization_barrier(grad_own.astype(jnp.bfloat16))
    rounded_other = lax.optimization_barrier(grad_other.astype(jnp.bfloat16))
    down_grad = (rounded_own.astype(jnp.float32) + rounded_other.astype(jnp.float32)).astype(
        jnp.bfloat16
    )
    hidden_float = hidden.astype(jnp.float32)
    score_head = jnp.sum(hidden_float[:, :moved] * (partial_own[:, :moved] + near), axis=1)
    score_head = score_head + jnp.sum(hidden_float[:, moved:] * partial_own[:, moved:], axis=1)
    partial_back, partial_own, near, down_grad, score_head = lax.optimization_barrier(
        (partial_back, partial_own, near, down_grad, score_head)
    )
    score = score_head + jnp.sum(hidden_float[:, moved:] * partial_back, axis=1)
    every_score = lax.all_gather(score, ("expert", "tensor"))
    upstream = partial_own + jnp.concatenate((near, partial_back), axis=1)
    hidden_grad = gate_column * upstream
    gate_grad = (hidden_grad * up_float * slope).astype(jnp.bfloat16)
    up_grad = (hidden_grad * active).astype(jnp.bfloat16)
    expert_here = lax.axis_index("expert")
    summed_scores = jnp.sum(every_score.reshape(expert_count, tensor_count, slots), axis=1)
    returned = lax.dynamic_slice_in_dim(
        summed_scores.reshape(expert_count, expert_count, capacity), expert_here, 1, axis=1
    )
    flat_scores = returned.reshape(-1)
    router_grad = jnp.stack(
        [
            jnp.sum(jnp.where(matches[which], flat_scores[None, :], 0.0), axis=1)
            for which in range(choices_each)
        ],
        axis=1,
    )
    return (gate_grad[None], up_grad[None], down_grad[None], router_grad)


def solution(mesh):
    placed = (
        P(("dp", "expert"), "tensor"),
        P(("dp", "expert"), None),
        P(("dp", "expert"), None),
        P("expert", "dp", "tensor"),
        P("expert", "dp", "tensor"),
        P("expert", "tensor", "dp"),
    )
    return jax.shard_map(
        local,
        mesh=mesh,
        in_specs=placed,
        out_specs=(
            P("expert", "dp", "tensor"),
            P("expert", "dp", "tensor"),
            P("expert", "tensor", "dp"),
            P(("dp", "expert"), None),
        ),
        check_vma=False,
    )
```

```python
import jax
import jax.numpy as jnp
from jax import lax
from jax.sharding import PartitionSpec as P

PARTIAL_DTYPE = jnp.bfloat16


def silu_parts(values):
    sigma = jax.nn.sigmoid(values)
    return (values * sigma, sigma * (1.0 + values * (1.0 - sigma)))


def swap_dp(value):
    return lax.ppermute(value, "dp", perm=[(0, 1), (1, 0)])


def local(output_grad, expert_ids, router_weights, gate_preact, up_preact, down_weight):
    expert_count = lax.axis_size("expert")
    tensor_count = lax.axis_size("tensor")
    replica = lax.axis_index("dp")
    part = lax.axis_index("tensor")
    tokens_here = expert_ids.shape[0]
    choices_each = expert_ids.shape[1]
    capacity = gate_preact.shape[1] // expert_count
    flat_ids = expert_ids.reshape(-1)
    one_hot = (flat_ids[:, None] == jnp.arange(expert_count, dtype=jnp.int32)).astype(jnp.int32)
    earlier = jnp.cumsum(one_hot, axis=0) - one_hot
    slot_index = jnp.sum(earlier * one_hot, axis=1)
    target = (flat_ids * capacity + slot_index).reshape(tokens_here, choices_each)
    columns = jnp.arange(expert_count * capacity, dtype=jnp.int32)
    matches = [target[:, which][:, None] == columns[None, :] for which in range(choices_each)]
    selector = jnp.zeros((tokens_here, expert_count * capacity), jnp.bfloat16)
    gate_table = jnp.zeros((tokens_here, expert_count * capacity), jnp.float32)
    for which in range(choices_each):
        selector = jnp.where(matches[which], jnp.bfloat16(1.0), selector)
        gate_table = jnp.where(
            matches[which], router_weights[:, which : which + 1].astype(jnp.float32), gate_table
        )
    gate_send = jnp.sum(gate_table, axis=0).astype(jnp.bfloat16).reshape(expert_count, capacity)

    local_weight = down_weight[0]
    units = local_weight.shape[0]
    moved = units * 3 // 16 // 128 * 128

    gate_float = gate_preact[0].astype(jnp.float32)
    up_float = up_preact[0].astype(jnp.float32)
    active, slope = silu_parts(gate_float)
    hidden = (active * up_float).astype(jnp.bfloat16)

    contract_rows = (((0,), (0,)), ((), ()))
    contract_cols = (((1,), (1,)), ((), ()))
    outgoing = lax.dot_general(
        selector, output_grad, contract_rows, preferred_element_type=jnp.float32
    )
    outgoing = outgoing.astype(jnp.bfloat16).reshape(expert_count, capacity, -1)
    hidden, outgoing, gate_send = lax.optimization_barrier((hidden, outgoing, gate_send))
    split = hidden.shape[0] // 2
    hidden_first = swap_dp(hidden[:split])
    gate_slots = lax.all_to_all(gate_send, "expert", split_axis=0, concat_axis=0, tiled=True)
    received = lax.all_to_all(outgoing, "expert", split_axis=0, concat_axis=0, tiled=True)
    slots = expert_count * capacity
    narrow_rows = received.reshape(slots, -1)
    gate_bf16 = gate_slots.reshape(-1)
    gate_column = gate_bf16.astype(jnp.float32)[:, None]
    other_gates = swap_dp(gate_bf16)
    narrow = narrow_rows.shape[1]
    cut = narrow // 2
    front = lax.all_gather(narrow_rows[:, :cut], "tensor", axis=1, tiled=True)
    back = lax.all_gather(narrow_rows[:, cut:], "tensor", axis=1, tiled=True)
    front, hidden_first, other_gates = lax.optimization_barrier(
        (front, hidden_first, other_gates)
    )

    width = narrow * tensor_count
    half = width // 2
    half_part = half // 2
    piece = half_part // tensor_count
    quarters = tensor_count // 2

    def in_order(front_part, back_part):
        blocks = []
        for quarter in range(quarters):
            blocks.append(front_part[:, quarter * cut : (quarter + 1) * cut])
            blocks.append(back_part[:, quarter * cut : (quarter + 1) * cut])
        return jnp.concatenate(blocks, axis=1)

    def half_of(rows, which):
        return lax.dynamic_slice_in_dim(rows, which * half_part, half_part, axis=1)

    send_front = lax.dynamic_slice_in_dim(
        front, (1 - replica) * half_part + part * piece, piece, axis=1
    )
    piece_front = swap_dp(send_front)
    hidden_rest, piece_front = lax.optimization_barrier((hidden[split:], piece_front))
    hidden_second = swap_dp(hidden_rest)
    send_back = lax.dynamic_slice_in_dim(
        back, (1 - replica) * half_part + part * piece, piece, axis=1
    )
    send_back, hidden_second = lax.optimization_barrier((send_back, hidden_second))
    piece_back = swap_dp(send_back)
    weight_rest, piece_back = lax.optimization_barrier((local_weight[:moved], piece_back))
    weight_moved = swap_dp(weight_rest)
    other_front = lax.all_gather(piece_front, "tensor", axis=1, tiled=True)
    other_front, front, back = lax.optimization_barrier((other_front, front, back))
    other_back = lax.all_gather(piece_back, "tensor", axis=1, tiled=True)
    other_rows = in_order(other_front, other_back)
    own_rows = in_order(half_of(front, replica), half_of(back, replica))
    far_rows = in_order(half_of(front, 1 - replica), half_of(back, 1 - replica))
    hidden_first, hidden_second, other_rows = lax.optimization_barrier(
        (hidden_first, hidden_second, other_rows)
    )
    other_gates = other_gates.astype(jnp.float32)[:, None]

    partial_other = lax.dot_general(
        other_rows, local_weight[moved:], contract_cols, preferred_element_type=jnp.float32
    )
    weight_moved, partial_send, hidden_first, hidden_second = lax.optimization_barrier(
        (weight_moved, partial_other.astype(PARTIAL_DTYPE), hidden_first, hidden_second)
    )
    partial_back = swap_dp(partial_send).astype(jnp.float32)
    partial_own = lax.dot_general(
        own_rows, local_weight, contract_cols, preferred_element_type=jnp.float32
    )
    near = lax.dot_general(far_rows, weight_moved, contract_cols, preferred_element_type=jnp.float32)

    scaled_own = (gate_column * own_rows.astype(jnp.float32)).astype(jnp.bfloat16)
    scaled_other = (other_gates * other_rows.astype(jnp.float32)).astype(jnp.bfloat16)
    grad_own = lax.dot_general(hidden, scaled_own, contract_rows, preferred_element_type=jnp.float32)
    hidden_other = jnp.concatenate((hidden_first, hidden_second), axis=0)
    grad_other = lax.dot_general(
        hidden_other, scaled_other, contract_rows, preferred_element_type=jnp.float32
    )
    rounded_own = lax.optimization_barrier(grad_own.astype(jnp.bfloat16))
    rounded_other = lax.optimization_barrier(grad_other.astype(jnp.bfloat16))
    down_grad = (rounded_own.astype(jnp.float32) + rounded_other.astype(jnp.float32)).astype(
        jnp.bfloat16
    )
    partial_back, partial_own, near, down_grad = lax.optimization_barrier(
        (partial_back, partial_own, near, down_grad)
    )
    upstream = partial_own + jnp.concatenate((near, partial_back), axis=1)

    score = jnp.sum(hidden.astype(jnp.float32) * upstream, axis=1)
    hidden_grad = gate_column * upstream
    gate_grad = (hidden_grad * up_float * slope).astype(jnp.bfloat16)
    up_grad = (hidden_grad * active).astype(jnp.bfloat16)
    summed_scores = lax.psum(score, "tensor")
    returned = lax.all_to_all(
        summed_scores.reshape(expert_count, capacity),
        "expert",
        split_axis=0,
        concat_axis=0,
        tiled=True,
    )
    flat_scores = returned.reshape(-1)
    router_grad = jnp.stack(
        [
            jnp.sum(jnp.where(matches[which], flat_scores[None, :], 0.0), axis=1)
            for which in range(choices_each)
        ],
        axis=1,
    )
    return (gate_grad[None], up_grad[None], down_grad[None], router_grad)


def solution(mesh):
    placed = (
        P(("dp", "expert"), "tensor"),
        P(("dp", "expert"), None),
        P(("dp", "expert"), None),
        P("expert", "dp", "tensor"),
        P("expert", "dp", "tensor"),
        P("expert", "tensor", "dp"),
    )
    return jax.shard_map(
        local,
        mesh=mesh,
        in_specs=placed,
        out_specs=(
            P("expert", "dp", "tensor"),
            P("expert", "dp", "tensor"),
            P("expert", "tensor", "dp"),
            P(("dp", "expert"), None),
        ),
        check_vma=False,
    )
```

```python
import jax
import jax.numpy as jnp
from jax import lax
from jax.sharding import PartitionSpec as P

PARTIAL_DTYPE = jnp.bfloat16


def silu_parts(values):
    sigma = jax.nn.sigmoid(values)
    return (values * sigma, sigma * (1.0 + values * (1.0 - sigma)))


def swap_dp(value):
    return lax.ppermute(value, "dp", perm=[(0, 1), (1, 0)])


def local(output_grad, expert_ids, router_weights, gate_preact, up_preact, down_weight):
    expert_count = lax.axis_size("expert")
    tensor_count = lax.axis_size("tensor")
    replica = lax.axis_index("dp")
    part = lax.axis_index("tensor")
    tokens_here = expert_ids.shape[0]
    choices_each = expert_ids.shape[1]
    capacity = gate_preact.shape[1] // expert_count
    flat_ids = expert_ids.reshape(-1)
    one_hot = (flat_ids[:, None] == jnp.arange(expert_count, dtype=jnp.int32)).astype(jnp.int32)
    earlier = jnp.cumsum(one_hot, axis=0) - one_hot
    slot_index = jnp.sum(earlier * one_hot, axis=1)
    target = (flat_ids * capacity + slot_index).reshape(tokens_here, choices_each)
    columns = jnp.arange(expert_count * capacity, dtype=jnp.int32)
    matches = [target[:, which][:, None] == columns[None, :] for which in range(choices_each)]
    selector = jnp.zeros((tokens_here, expert_count * capacity), jnp.bfloat16)
    gate_table = jnp.zeros((tokens_here, expert_count * capacity), jnp.float32)
    for which in range(choices_each):
        selector = jnp.where(matches[which], jnp.bfloat16(1.0), selector)
        gate_table = jnp.where(
            matches[which], router_weights[:, which : which + 1].astype(jnp.float32), gate_table
        )
    gate_send = jnp.sum(gate_table, axis=0).astype(jnp.bfloat16).reshape(expert_count, capacity)

    local_weight = down_weight[0]
    units = local_weight.shape[0]
    moved = units // 4 // 16 * 16

    gate_float = gate_preact[0].astype(jnp.float32)
    up_float = up_preact[0].astype(jnp.float32)
    active, slope = silu_parts(gate_float)
    hidden = (active * up_float).astype(jnp.bfloat16)

    contract_rows = (((0,), (0,)), ((), ()))
    contract_cols = (((1,), (1,)), ((), ()))
    outgoing = lax.dot_general(
        selector, output_grad, contract_rows, preferred_element_type=jnp.float32
    )
    outgoing = outgoing.astype(jnp.bfloat16).reshape(expert_count, capacity, -1)
    hidden, outgoing, gate_send = lax.optimization_barrier((hidden, outgoing, gate_send))
    hidden_other = swap_dp(hidden)
    gate_slots = lax.all_to_all(gate_send, "expert", split_axis=0, concat_axis=0, tiled=True)
    received = lax.all_to_all(outgoing, "expert", split_axis=0, concat_axis=0, tiled=True)
    slots = expert_count * capacity
    narrow_rows = received.reshape(slots, -1)
    gate_bf16 = gate_slots.reshape(-1)
    gate_column = gate_bf16.astype(jnp.float32)[:, None]
    other_gates = swap_dp(gate_bf16)
    fragment = lax.all_gather(narrow_rows, "tensor", axis=1, tiled=True)
    fragment, hidden_other, other_gates = lax.optimization_barrier(
        (fragment, hidden_other, other_gates)
    )

    width = fragment.shape[1]
    half = width // 2
    piece = half // tensor_count
    own_rows = lax.dynamic_slice_in_dim(fragment, replica * half, half, axis=1)
    send_rows = lax.dynamic_slice_in_dim(
        fragment, (1 - replica) * half + part * piece, piece, axis=1
    )
    other_piece = swap_dp(send_rows)
    weight_rest, other_piece = lax.optimization_barrier((local_weight[:moved], other_piece))
    weight_moved = swap_dp(weight_rest)
    other_rows = lax.all_gather(other_piece, "tensor", axis=1, tiled=True)
    hidden_other, other_rows = lax.optimization_barrier((hidden_other, other_rows))
    other_gates = other_gates.astype(jnp.float32)[:, None]

    partial_other = lax.dot_general(
        other_rows, local_weight[moved:], contract_cols, preferred_element_type=jnp.float32
    )
    weight_moved, partial_send, own_rows = lax.optimization_barrier(
        (weight_moved, partial_other.astype(PARTIAL_DTYPE), own_rows)
    )
    partial_back = swap_dp(partial_send).astype(jnp.float32)
    partial_own = lax.dot_general(
        own_rows, local_weight, contract_cols, preferred_element_type=jnp.float32
    )
    far_rows = lax.dynamic_slice_in_dim(fragment, (1 - replica) * half, half, axis=1)
    near = lax.dot_general(far_rows, weight_moved, contract_cols, preferred_element_type=jnp.float32)

    scaled_own = (gate_column * own_rows.astype(jnp.float32)).astype(jnp.bfloat16)
    scaled_other = (other_gates * other_rows.astype(jnp.float32)).astype(jnp.bfloat16)
    grad_own = lax.dot_general(hidden, scaled_own, contract_rows, preferred_element_type=jnp.float32)
    grad_other = lax.dot_general(
        hidden_other, scaled_other, contract_rows, preferred_element_type=jnp.float32
    )
    rounded_own = lax.optimization_barrier(grad_own.astype(jnp.bfloat16))
    rounded_other = lax.optimization_barrier(grad_other.astype(jnp.bfloat16))
    down_grad = (rounded_own.astype(jnp.float32) + rounded_other.astype(jnp.float32)).astype(
        jnp.bfloat16
    )
    partial_back, partial_own, near, down_grad = lax.optimization_barrier(
        (partial_back, partial_own, near, down_grad)
    )
    upstream = partial_own + jnp.concatenate((near, partial_back), axis=1)
    score = jnp.sum(hidden.astype(jnp.float32) * upstream, axis=1)
    score, partial_back = lax.optimization_barrier((score, partial_back))
    every_score = lax.all_gather(score, "tensor")
    upstream = partial_own + jnp.concatenate((near, partial_back), axis=1)
    hidden_grad = gate_column * upstream
    gate_grad = (hidden_grad * up_float * slope).astype(jnp.bfloat16)
    up_grad = (hidden_grad * active).astype(jnp.bfloat16)
    summed_scores = jnp.sum(every_score, axis=0)
    returned = lax.all_to_all(
        summed_scores.reshape(expert_count, capacity),
        "expert",
        split_axis=0,
        concat_axis=0,
        tiled=True,
    )
    flat_scores = returned.reshape(-1)
    router_grad = jnp.stack(
        [
            jnp.sum(jnp.where(matches[which], flat_scores[None, :], 0.0), axis=1)
            for which in range(choices_each)
        ],
        axis=1,
    )
    return (gate_grad[None], up_grad[None], down_grad[None], router_grad)


def solution(mesh):
    placed = (
        P(("dp", "expert"), "tensor"),
        P(("dp", "expert"), None),
        P(("dp", "expert"), None),
        P("expert", "dp", "tensor"),
        P("expert", "dp", "tensor"),
        P("expert", "tensor", "dp"),
    )
    return jax.shard_map(
        local,
        mesh=mesh,
        in_specs=placed,
        out_specs=(
            P("expert", "dp", "tensor"),
            P("expert", "dp", "tensor"),
            P("expert", "tensor", "dp"),
            P(("dp", "expert"), None),
        ),
        check_vma=False,
    )
```

```python
import jax
import jax.numpy as jnp
from jax import lax
from jax.sharding import PartitionSpec as P

PARTIAL_DTYPE = jnp.bfloat16


def silu_parts(values):
    sigma = jax.nn.sigmoid(values)
    return (values * sigma, sigma * (1.0 + values * (1.0 - sigma)))


def swap_dp(value):
    return lax.ppermute(value, "dp", perm=[(0, 1), (1, 0)])


def local(output_grad, expert_ids, router_weights, gate_preact, up_preact, down_weight):
    expert_count = lax.axis_size("expert")
    tensor_count = lax.axis_size("tensor")
    replica = lax.axis_index("dp")
    part = lax.axis_index("tensor")
    tokens_here = expert_ids.shape[0]
    choices_each = expert_ids.shape[1]
    capacity = gate_preact.shape[1] // expert_count
    flat_ids = expert_ids.reshape(-1)
    one_hot = (flat_ids[:, None] == jnp.arange(expert_count, dtype=jnp.int32)).astype(jnp.int32)
    earlier = jnp.cumsum(one_hot, axis=0) - one_hot
    slot_index = jnp.sum(earlier * one_hot, axis=1)
    target = (flat_ids * capacity + slot_index).reshape(tokens_here, choices_each)
    columns = jnp.arange(expert_count * capacity, dtype=jnp.int32)
    matches = [target[:, which][:, None] == columns[None, :] for which in range(choices_each)]
    selector = jnp.zeros((tokens_here, expert_count * capacity), jnp.bfloat16)
    gate_table = jnp.zeros((tokens_here, expert_count * capacity), jnp.float32)
    for which in range(choices_each):
        selector = jnp.where(matches[which], jnp.bfloat16(1.0), selector)
        gate_table = jnp.where(
            matches[which], router_weights[:, which : which + 1].astype(jnp.float32), gate_table
        )
    gate_send = jnp.sum(gate_table, axis=0).astype(jnp.bfloat16).reshape(expert_count, capacity)

    local_weight = down_weight[0]

    gate_float = gate_preact[0].astype(jnp.float32)
    up_float = up_preact[0].astype(jnp.float32)
    active, slope = silu_parts(gate_float)
    hidden = (active * up_float).astype(jnp.bfloat16)

    contract_rows = (((0,), (0,)), ((), ()))
    contract_cols = (((1,), (1,)), ((), ()))
    outgoing = lax.dot_general(
        selector, output_grad, contract_rows, preferred_element_type=jnp.float32
    )
    outgoing = outgoing.astype(jnp.bfloat16).reshape(expert_count, capacity, -1)
    hidden, outgoing, gate_send = lax.optimization_barrier((hidden, outgoing, gate_send))
    gate_slots = lax.all_to_all(gate_send, "expert", split_axis=0, concat_axis=0, tiled=True)
    received = lax.all_to_all(outgoing, "expert", split_axis=0, concat_axis=0, tiled=True)
    slots = expert_count * capacity
    narrow_rows = received.reshape(slots, -1)
    gate_bf16 = gate_slots.reshape(-1)
    gate_column = gate_bf16.astype(jnp.float32)[:, None]
    other_gates = swap_dp(gate_bf16)
    narrow = narrow_rows.shape[1]
    width = narrow * tensor_count
    half = width // 2
    quarters = tensor_count // 2
    chunk = narrow // tensor_count
    mixed = lax.all_to_all(narrow_rows, "tensor", split_axis=1, concat_axis=1, tiled=True)
    send_rows = lax.dynamic_slice_in_dim(mixed, (1 - replica) * (narrow // 2), narrow // 2, axis=1)
    other_piece = swap_dp(send_rows)
    hidden_send, other_piece, other_gates = lax.optimization_barrier(
        (hidden, other_piece, other_gates)
    )
    hidden_other = swap_dp(hidden_send)
    gathered = lax.all_gather(other_piece, "tensor", axis=1, tiled=True)
    rows_for_gather, gathered = lax.optimization_barrier((narrow_rows, gathered))
    fragment = lax.all_gather(rows_for_gather, "tensor", axis=1, tiled=True)
    gathered, hidden_other = lax.optimization_barrier((gathered, hidden_other))
    blocks = []
    for quarter in range(quarters):
        for source in range(tensor_count):
            begin = source * (narrow // 2) + quarter * chunk
            blocks.append(gathered[:, begin : begin + chunk])
    other_rows = jnp.concatenate(blocks, axis=1)
    own_rows = lax.dynamic_slice_in_dim(fragment, replica * half, half, axis=1)
    other_gates = other_gates.astype(jnp.float32)[:, None]

    partial_other = lax.dot_general(
        other_rows, local_weight, contract_cols, preferred_element_type=jnp.float32
    )
    units = local_weight.shape[0]
    first_units = units // 2 // 128 * 128
    partial_first = swap_dp(partial_other[:, :first_units].astype(PARTIAL_DTYPE))
    partial_own = lax.dot_general(
        own_rows, local_weight, contract_cols, preferred_element_type=jnp.float32
    )

    scaled_own = (gate_column * own_rows.astype(jnp.float32)).astype(jnp.bfloat16)
    scaled_other = (other_gates * other_rows.astype(jnp.float32)).astype(jnp.bfloat16)
    grad_own = lax.dot_general(hidden, scaled_own, contract_rows, preferred_element_type=jnp.float32)
    grad_other = lax.dot_general(
        hidden_other, scaled_other, contract_rows, preferred_element_type=jnp.float32
    )
    rounded_own = lax.optimization_barrier(grad_own.astype(jnp.bfloat16))
    partial_rest, partial_own, rounded_own = lax.optimization_barrier(
        (partial_other[:, first_units:].astype(PARTIAL_DTYPE), partial_own, rounded_own)
    )
    partial_second = swap_dp(partial_rest)
    rounded_other = lax.optimization_barrier(grad_other.astype(jnp.bfloat16))
    down_grad = (rounded_own.astype(jnp.float32) + rounded_other.astype(jnp.float32)).astype(
        jnp.bfloat16
    )
    partial_first, partial_second, partial_own, down_grad = lax.optimization_barrier(
        (partial_first, partial_second, partial_own, down_grad)
    )
    partial_back = jnp.concatenate((partial_first, partial_second), axis=1).astype(jnp.float32)
    upstream = partial_own + partial_back

    score = jnp.sum(hidden.astype(jnp.float32) * upstream, axis=1)
    hidden_grad = gate_column * upstream
    gate_grad = (hidden_grad * up_float * slope).astype(jnp.bfloat16)
    up_grad = (hidden_grad * active).astype(jnp.bfloat16)
    summed_scores = lax.psum(score, "tensor")
    returned = lax.all_to_all(
        summed_scores.reshape(expert_count, capacity),
        "expert",
        split_axis=0,
        concat_axis=0,
        tiled=True,
    )
    flat_scores = returned.reshape(-1)
    router_grad = jnp.stack(
        [
            jnp.sum(jnp.where(matches[which], flat_scores[None, :], 0.0), axis=1)
            for which in range(choices_each)
        ],
        axis=1,
    )
    return (gate_grad[None], up_grad[None], down_grad[None], router_grad)


def solution(mesh):
    placed = (
        P(("dp", "expert"), "tensor"),
        P(("dp", "expert"), None),
        P(("dp", "expert"), None),
        P("expert", "dp", "tensor"),
        P("expert", "dp", "tensor"),
        P("expert", "tensor", "dp"),
    )
    return jax.shard_map(
        local,
        mesh=mesh,
        in_specs=placed,
        out_specs=(
            P("expert", "dp", "tensor"),
            P("expert", "dp", "tensor"),
            P("expert", "tensor", "dp"),
            P(("dp", "expert"), None),
        ),
        check_vma=False,
    )
```

```python
import jax
import jax.numpy as jnp
from jax import lax
from jax.sharding import PartitionSpec as P

PARTIAL_DTYPE = jnp.bfloat16


def silu_parts(values):
    sigma = jax.nn.sigmoid(values)
    return (values * sigma, sigma * (1.0 + values * (1.0 - sigma)))


def swap_dp(value):
    return lax.ppermute(value, "dp", perm=[(0, 1), (1, 0)])


def local(output_grad, expert_ids, router_weights, gate_preact, up_preact, down_weight):
    expert_count = lax.axis_size("expert")
    tensor_count = lax.axis_size("tensor")
    replica = lax.axis_index("dp")
    part = lax.axis_index("tensor")
    tokens_here = expert_ids.shape[0]
    choices_each = expert_ids.shape[1]
    capacity = gate_preact.shape[1] // expert_count
    flat_ids = expert_ids.reshape(-1)
    one_hot = (flat_ids[:, None] == jnp.arange(expert_count, dtype=jnp.int32)).astype(jnp.int32)
    earlier = jnp.cumsum(one_hot, axis=0) - one_hot
    slot_index = jnp.sum(earlier * one_hot, axis=1)
    target = (flat_ids * capacity + slot_index).reshape(tokens_here, choices_each)
    columns = jnp.arange(expert_count * capacity, dtype=jnp.int32)
    matches = [target[:, which][:, None] == columns[None, :] for which in range(choices_each)]
    selector = jnp.zeros((tokens_here, expert_count * capacity), jnp.bfloat16)
    gate_table = jnp.zeros((tokens_here, expert_count * capacity), jnp.float32)
    for which in range(choices_each):
        selector = jnp.where(matches[which], jnp.bfloat16(1.0), selector)
        gate_table = jnp.where(
            matches[which], router_weights[:, which : which + 1].astype(jnp.float32), gate_table
        )
    gate_send = jnp.sum(gate_table, axis=0).astype(jnp.bfloat16).reshape(expert_count, capacity)

    local_weight = down_weight[0]
    units = local_weight.shape[0]
    moved = units * 2 // 7 // 128 * 128

    gate_float = gate_preact[0].astype(jnp.float32)
    up_float = up_preact[0].astype(jnp.float32)
    active, slope = silu_parts(gate_float)
    hidden = (active * up_float).astype(jnp.bfloat16)

    contract_rows = (((0,), (0,)), ((), ()))
    contract_cols = (((1,), (1,)), ((), ()))
    outgoing = lax.dot_general(
        selector, output_grad, contract_rows, preferred_element_type=jnp.float32
    )
    outgoing = outgoing.astype(jnp.bfloat16).reshape(expert_count, capacity, -1)
    hidden, outgoing, gate_send = lax.optimization_barrier((hidden, outgoing, gate_send))
    hidden_other = swap_dp(hidden)
    gate_slots = lax.all_to_all(gate_send, "expert", split_axis=0, concat_axis=0, tiled=True)
    received = lax.all_to_all(outgoing, "expert", split_axis=0, concat_axis=0, tiled=True)
    slots = expert_count * capacity
    narrow_rows = received.reshape(slots, -1)
    gate_bf16 = gate_slots.reshape(-1)
    gate_column = gate_bf16.astype(jnp.float32)[:, None]
    other_gates = swap_dp(gate_bf16)
    fragment = lax.all_gather(narrow_rows, "tensor", axis=1, tiled=True)
    fragment, hidden_other, other_gates = lax.optimization_barrier(
        (fragment, hidden_other, other_gates)
    )

    width = fragment.shape[1]
    half = width // 2
    piece = half // tensor_count
    own_rows = lax.dynamic_slice_in_dim(fragment, replica * half, half, axis=1)
    send_rows = lax.dynamic_slice_in_dim(
        fragment, (1 - replica) * half + part * piece, piece, axis=1
    )
    other_piece = swap_dp(send_rows)
    weight_rest, other_piece = lax.optimization_barrier((local_weight[:moved], other_piece))
    weight_moved = swap_dp(weight_rest)
    other_rows = lax.all_gather(other_piece, "tensor", axis=1, tiled=True)
    hidden_other, other_rows = lax.optimization_barrier((hidden_other, other_rows))
    other_gates = other_gates.astype(jnp.float32)[:, None]

    partial_other = lax.dot_general(
        other_rows, local_weight[moved:], contract_cols, preferred_element_type=jnp.float32
    )
    weight_moved, partial_send, own_rows = lax.optimization_barrier(
        (weight_moved, partial_other.astype(PARTIAL_DTYPE), own_rows)
    )
    partial_back = swap_dp(partial_send).astype(jnp.float32)
    partial_own = lax.dot_general(
        own_rows, local_weight, contract_cols, preferred_element_type=jnp.float32
    )
    far_rows = lax.dynamic_slice_in_dim(fragment, (1 - replica) * half, half, axis=1)
    near = lax.dot_general(far_rows, weight_moved, contract_cols, preferred_element_type=jnp.float32)

    scaled_own = (gate_column * own_rows.astype(jnp.float32)).astype(jnp.bfloat16)
    scaled_other = (other_gates * other_rows.astype(jnp.float32)).astype(jnp.bfloat16)
    grad_own = lax.dot_general(hidden, scaled_own, contract_rows, preferred_element_type=jnp.float32)
    grad_other = lax.dot_general(
        hidden_other, scaled_other, contract_rows, preferred_element_type=jnp.float32
    )
    rounded_own = lax.optimization_barrier(grad_own.astype(jnp.bfloat16))
    rounded_other = lax.optimization_barrier(grad_other.astype(jnp.bfloat16))
    down_grad = (rounded_own.astype(jnp.float32) + rounded_other.astype(jnp.float32)).astype(
        jnp.bfloat16
    )
    partial_back, partial_own, near, down_grad = lax.optimization_barrier(
        (partial_back, partial_own, near, down_grad)
    )
    upstream = partial_own + jnp.concatenate((near, partial_back), axis=1)

    score = jnp.sum(hidden.astype(jnp.float32) * upstream, axis=1)
    hidden_grad = gate_column * upstream
    gate_grad = (hidden_grad * up_float * slope).astype(jnp.bfloat16)
    up_grad = (hidden_grad * active).astype(jnp.bfloat16)
    summed_scores = lax.psum(score, "tensor")
    returned = lax.all_to_all(
        summed_scores.reshape(expert_count, capacity),
        "expert",
        split_axis=0,
        concat_axis=0,
        tiled=True,
    )
    flat_scores = returned.reshape(-1)
    router_grad = jnp.stack(
        [
            jnp.sum(jnp.where(matches[which], flat_scores[None, :], 0.0), axis=1)
            for which in range(choices_each)
        ],
        axis=1,
    )
    return (gate_grad[None], up_grad[None], down_grad[None], router_grad)


def solution(mesh):
    placed = (
        P(("dp", "expert"), "tensor"),
        P(("dp", "expert"), None),
        P(("dp", "expert"), None),
        P("expert", "dp", "tensor"),
        P("expert", "dp", "tensor"),
        P("expert", "tensor", "dp"),
    )
    return jax.shard_map(
        local,
        mesh=mesh,
        in_specs=placed,
        out_specs=(
            P("expert", "dp", "tensor"),
            P("expert", "dp", "tensor"),
            P("expert", "tensor", "dp"),
            P(("dp", "expert"), None),
        ),
        check_vma=False,
    )
```
